768 devices in a mesh: dp: 12 (over z), phase: 4 (over x), ctx: 16 (over y, core).
Axes of the slice: x: 4, y: 8, z: 12, core: 2. Of those that a mesh axis runs over, the one named last changes fastest.
Arguments:
- queries: bfloat16 [12, 4096, 4096], P('dp', 'ctx', 'phase'), may hold values from -6 to 6
- keys: bfloat16 [12, 4096, 512], P('dp', 'ctx', 'phase'), may hold values from -6 to 6
- values: bfloat16 [12, 4096, 512], P('dp', 'ctx', 'phase'), may hold values from -6 to 6
- segment_ids: int32 [12, 4096], P('dp', 'ctx'), may hold values from 0 to 7, never falling along the last dimension, each value on 1 to 1024 neighbouring positions
- span_ids: int32 [12, 4096], P('dp', 'ctx'), may hold values from 0 to 2, as said below
- readout: float32 [4096], P('phase'), may hold values from -6 to 6
Outputs:
- attended: bfloat16 [12, 4096, 4096], P('dp', 'ctx', 'phase')
- span_scores: float32 [12, 2], P('dp')
- pair_loss: float32 [], replicated
The draws below stay inside these ranges and needn't reach their ends.
Inputs may be any that keep to these rules, and one draw needn't show every extreme that they name: `segment_ids`: segment ids never fall along a sequence; each segment covers at most 1024 positions, and some segment covers exactly that many. `span_ids`: positions labelled 1 form one contiguous run, and positions labelled 2 form one later contiguous run.
All inputs are finite; a program needn't handle non-finite values.
Results may differ from the reference program's by a relative error of at most 0.0036.
Values may be sent and summed in bfloat16 or wider, within the bound.
No kernel may reach another device: no remote copies, remote signals or barrier semaphores. Data moves between devices by JAX's collectives and lax.ppermute only.
A program may use at most 128 MiB of HBM per device.

```python
import math
import jax
import jax.numpy as jnp
import numpy as np
from jax import lax

HD = 128
QPK = 8
KVH = 4
HEADS = 32
SEQ = 4096
SEQS = 12


def plant_layout(key):
    layout_key = jax.random.fold_in(key, 7177)
    pick_key, sign_key = jax.random.split(layout_key)
    quarter = SEQ // 4
    offsets = jax.random.randint(pick_key, (SEQS, 4), 2, quarter)
    points = offsets + (jnp.arange(4) * quarter)[None, :]
    position = jnp.arange(SEQ)
    planted = jnp.any(position[None, :, None] == points[:, None, :], axis=-1)
    preceding = jnp.any(position[None, :, None] + 1 == points[:, None, :], axis=-1)
    coins = jax.random.bernoulli(sign_key, 0.5, (SEQS, SEQ, KVH, HD))
    sign_field = jnp.where(coins, 1.0, -1.0).astype(jnp.float32)
    return (planted, preceding, sign_field)


def draw_queries(key, part):
    planted, preceding, sign_field = plant_layout(key)
    noise_key = jax.random.fold_in(key, 11)
    level_key = jax.random.fold_in(key, 53)
    full_shape = (SEQS, SEQ, KVH, QPK, HD)
    noise_field = jnp.clip(jax.random.normal(noise_key, full_shape, jnp.float32), -6.0, 6.0)
    levels = jax.random.randint(level_key, (SEQS, SEQ, KVH, QPK, 1), 0, 4).astype(jnp.float32)
    strength = 4.5 + 0.5 * levels
    aligned = strength * sign_field[:, :, :, None, :]
    result = jnp.where(planted[:, :, None, None, None], aligned, noise_field)
    return result.reshape(SEQS, SEQ, HEADS * HD).astype(jnp.bfloat16)


def draw_keys(key, part):
    planted, preceding, sign_field = plant_layout(key)
    noise_key = jax.random.fold_in(key, 29)
    full_shape = (SEQS, SEQ, KVH, HD)
    noise_field = jnp.clip(jax.random.normal(noise_key, full_shape, jnp.float32), -6.0, 6.0)
    following = jnp.roll(sign_field, -1, axis=1)
    lowered = jnp.where(jnp.arange(HD) < max(1, HD // 64), 1.75, 3.5).astype(jnp.float32)
    near_copy = following * lowered[None, None, None, :]
    result = jnp.where(planted[:, :, None, None], 3.5 * sign_field, jnp.where(preceding[:, :, None, None], near_copy, noise_field))
    return result.reshape(SEQS, SEQ, KVH * HD).astype(jnp.bfloat16)


def draw_span_ids(key, part):
    first_key, second_key, third_key, fourth_key = jax.random.split(jax.random.fold_in(key, 97), 4)
    position = jnp.arange(SEQ)[None, :]
    chosen_start = jax.random.randint(first_key, (SEQS, 1), SEQ // 16, SEQ // 8)
    chosen_length = jax.random.randint(second_key, (SEQS, 1), SEQ // 4, 3 * SEQ // 8 + 1)
    reject_start = SEQ // 2 + jax.random.randint(third_key, (SEQS, 1), SEQ // 16, SEQ // 8)
    reject_length = jax.random.randint(fourth_key, (SEQS, 1), SEQ // 4, 3 * SEQ // 8 + 1)
    chosen = (position >= chosen_start) & (position < chosen_start + chosen_length)
    reject = (position >= reject_start) & (position < reject_start + reject_length)
    return jnp.where(chosen, 1, jnp.where(reject, 2, 0)).astype(jnp.int32)


def block_levels(rng, extent, shards, least, top_value):
    gain, own = 1.0, jax.random.fold_in(rng, 6)
    for axis_at, parts in shards:
        steps = jnp.exp(jax.random.uniform(jax.random.fold_in(own, axis_at), (parts,), jnp.float32, least / len(shards), top_value / len(shards)))
        gain = gain * jnp.repeat(steps, extent[axis_at] // parts).reshape([-1 if axis == axis_at else 1 for axis in range(len(extent))])
    return gain


def length_profile(count, total, bound, lean):
    loads = [(1 << 20) // math.isqrt(grade ** lean) + 1 for grade in range(2, count + 1)]
    rest, given = total - bound - (count - 1), [1] * (count - 1)
    while rest > 0:
        free = [i for i in range(count - 1) if given[i] < bound]
        mass, budget = sum([loads[i] for i in free]), rest
        for i in free:
            addition = min(bound - given[i], max(1, budget * loads[i] // mass), rest)
            given[i] = given[i] + addition
            rest = rest - addition
    return np.array([bound] + given)


def uneven_parts(rng, count, total, most, slope):
    if count == 2:
        one = jax.random.randint(rng, (), max(1, total - most), min(most, total - 1) + 1)
        return jnp.stack([one, total - one])
    lengths = jnp.asarray(length_profile(count, total, most, slope), jnp.int32)
    couples = (count - 1) // 2
    donor, taker = lengths[1:1 + 2 * couples:2], lengths[2:2 + 2 * couples:2]
    room = jnp.minimum(donor - 1, most - taker)
    shifted = jax.random.randint(jax.random.fold_in(rng, 1), (couples,), 0, 1 << 20) % (room + 1)
    lengths = lengths.at[1:1 + 2 * couples:2].set(donor - shifted).at[2:2 + 2 * couples:2].set(taker + shifted)
    return lengths[jax.random.permutation(jax.random.fold_in(rng, 2), count)]


def normal_values(rng, dims, scale, limit, pieces=(), dtype=jnp.bfloat16):
    values = jax.random.normal(rng, dims, jnp.float32) * scale
    if len(pieces) > 0:
        values = block_levels(rng, dims, pieces, -0.22, 0.18) * values
    return jnp.clip(values, min=-limit, max=limit).astype(dtype)


def setup_inputs(seed: int = 0) -> dict:
    splits = jax.random.split(jax.random.key(seed), 7)
    queries = draw_queries(jax.random.fold_in(splits[6], 71), 0)
    keys = draw_keys(jax.random.fold_in(splits[6], 71), 0)
    values = normal_values(splits[2], (SEQS, SEQ, KVH * HD), 1.0, 6.0, ((0, 12), (1, 16), (2, 4)))
    segment_ids = jax.vmap(lambda own: jnp.searchsorted(jnp.cumsum(uneven_parts(own, 8, SEQ, SEQ // 4, 2)), jnp.arange(SEQ), side="right"))(jax.random.split(splits[3], SEQS)).reshape((SEQS, SEQ)).astype(jnp.int32)
    span_ids = draw_span_ids(jax.random.fold_in(splits[6], 71), 0)
    readout = normal_values(splits[5], (HEADS * HD,), 1.0, 6.0, ((0, 4),), jnp.float32)
    return dict(queries=queries, keys=keys, values=values, segment_ids=segment_ids, span_ids=span_ids, readout=readout)


def one_seq(args):
    qs, ks, vs, segs, spans, readout = args
    pos = jnp.arange(SEQ)
    rows = 512 if SEQ % 512 == 0 else SEQ
    qb = qs.reshape(SEQ // rows, rows, HEADS, HD)

    def block(item):
        qblk, start = item
        qpos = start + jnp.arange(rows)
        qseg = lax.dynamic_slice_in_dim(segs, start, rows)
        allow = (pos[None, :] <= qpos[:, None]) & (segs[None, :] == qseg[:, None])
        outs = []
        for g in range(KVH):
            qh = qblk[:, g * QPK:(g + 1) * QPK, :].astype(jnp.float32)
            kh = ks[:, g * HD:(g + 1) * HD].astype(jnp.float32)
            vh = vs[:, g * HD:(g + 1) * HD].astype(jnp.float32)
            sc = jnp.einsum('ihd,jd->hij', qh, kh) / jnp.sqrt(jnp.float32(HD))
            sc = jnp.where(allow[None], sc, jnp.float32(-1e+30))
            top = lax.optimization_barrier(jnp.max(sc, axis=-1, keepdims=True))
            prob = jnp.where(allow[None], jnp.exp(sc - top), 0.0)
            total = lax.optimization_barrier(jnp.sum(prob, axis=-1))
            wts = prob.astype(jnp.bfloat16).astype(jnp.float32)
            acc = jnp.einsum('hij,jd->ihd', wts, vh)
            outs.append(acc / jnp.transpose(total)[:, :, None])
        return jnp.concatenate(outs, axis=1).reshape(rows, HEADS * HD)
    starts = (jnp.arange(SEQ // rows) * rows).astype(jnp.int32)
    full = lax.map(block, (qb, starts)).reshape(SEQ, HEADS * HD)
    score = lax.optimization_barrier(jnp.sum(full * readout[None, :], axis=1))
    chosen = jnp.sum(jnp.where(spans == 1, score, 0.0)) / 64.0
    reject = jnp.sum(jnp.where(spans == 2, score, 0.0)) / 64.0
    return (full.astype(jnp.bfloat16), jnp.stack([chosen, reject]))

def reference(queries, keys, values, segment_ids, span_ids, readout):
    reps = jnp.broadcast_to(readout, (SEQS, HEADS * HD))
    attended, span_scores = lax.map(one_seq, (queries, keys, values, segment_ids, span_ids, reps))
    pair_loss = jnp.mean(jax.nn.softplus(-(span_scores[:, 0] - span_scores[:, 1])))
    return (attended, span_scores, pair_loss)
```

```python
import jax
import jax.numpy as jnp
from jax import lax
from jax.sharding import PartitionSpec as P

MAX_SEGMENT = 1024


def per_device(queries, keys, values, segment_ids, span_ids, readout):
    tok = queries.shape[1]
    head_dim = keys.shape[2]
    heads = queries.shape[2] // head_dim
    n_ctx = lax.axis_size("ctx")
    back = min((MAX_SEGMENT - 1 + tok - 1) // tok, n_ctx - 1)
    here = lax.axis_index("ctx")
    qseg = segment_ids[0]
    qpos = here * tok + jnp.arange(tok)

    kv = jnp.concatenate([keys[0], values[0]], axis=1)
    segrow = jnp.broadcast_to(qseg.astype(jnp.bfloat16)[None, :], (16, tok))
    segrow = jnp.pad(segrow, ((0, 0), (0, 2 * head_dim - tok))) if tok < 2 * head_dim else segrow[:, : 2 * head_dim]
    packed = jnp.concatenate([kv, segrow], axis=0)
    pieces = []
    for d in range(back, 0, -1):
        pairs = [(i, i + d) for i in range(n_ctx - d)]
        pieces.append(lax.ppermute(packed, "ctx", pairs))
    pieces.append(packed)
    kall = jnp.concatenate([p[:tok, :head_dim] for p in pieces], axis=0)
    vall = jnp.concatenate([p[:tok, head_dim:] for p in pieces], axis=0)
    sall = jnp.concatenate([p[tok, :tok] for p in pieces], axis=0).astype(jnp.float32)
    kpos = (here - back) * tok + jnp.arange((back + 1) * tok)

    allow = (
        (kpos[None, :] <= qpos[:, None])
        & (kpos[None, :] >= 0)
        & (sall[None, :] == qseg.astype(jnp.float32)[:, None])
    )
    q3 = queries[0].reshape(tok, heads, head_dim)
    sc = jnp.einsum("ihd,jd->ihj", q3, kall, preferred_element_type=jnp.float32)
    sc = jnp.where(allow[:, None, :], sc / jnp.sqrt(jnp.float32(head_dim)), jnp.float32(-1e30))
    top = jnp.max(sc, axis=-1, keepdims=True)
    prob = jnp.where(allow[:, None, :], jnp.exp(sc - top), 0.0)
    total = jnp.sum(prob, axis=-1)
    acc = jnp.einsum(
        "ihj,jd->ihd", prob.astype(jnp.bfloat16), vall, preferred_element_type=jnp.float32
    )
    flat = (acc / total[:, :, None]).reshape(tok, heads * head_dim)
    attended = flat.astype(jnp.bfloat16)[None]
    score = jnp.sum(flat * readout[None, :], axis=1)
    spans = span_ids[0]
    partial_value = (
        jnp.stack(
            [jnp.sum(jnp.where(spans == 1, score, 0.0)), jnp.sum(jnp.where(spans == 2, score, 0.0))]
        )
        / 64.0
    )
    span_scores = lax.psum(lax.all_gather(partial_value, "ctx").sum(0), "phase")
    every = lax.all_gather(span_scores, "dp")
    pair_loss = jnp.mean(jax.nn.softplus(-(every[:, 0] - every[:, 1])))
    return (attended, span_scores[None], pair_loss)


def solution(mesh):
    in_specs = (
        P("dp", "ctx", "phase"),
        P("dp", "ctx", "phase"),
        P("dp", "ctx", "phase"),
        P("dp", "ctx"),
        P("dp", "ctx"),
        P("phase"),
    )
    out_specs = (P("dp", "ctx", "phase"), P("dp", None), P())
    return jax.shard_map(
        per_device, mesh=mesh, in_specs=in_specs, out_specs=out_specs, check_vma=False
    )
```

```python
import functools
import jax
import jax.numpy as jnp
from jax import lax
from jax.experimental import pallas as pl
from jax.experimental.pallas import tpu as pltpu
from jax.sharding import PartitionSpec as P

MAX_SEGMENT = 1024


def attend_kernel(q_ref, k_ref, v_ref, qpos_ref, qseg_ref, kpos_ref, kseg_ref, r_ref, o_ref, s_ref):
    h = pl.program_id(0)
    allow = (
        (kpos_ref[...] <= qpos_ref[...])
        & (kpos_ref[...] >= 0)
        & (kseg_ref[...] == qseg_ref[...])
    )
    scale = 1.0 / jnp.sqrt(jnp.float32(q_ref.shape[1]))
    sc = lax.dot_general(
        q_ref[...], k_ref[...], (((1,), (1,)), ((), ())), preferred_element_type=jnp.float32
    )
    sc = jnp.where(allow, sc * scale, jnp.float32(-1e30))
    top = jnp.max(sc, axis=1, keepdims=True)
    prob = jnp.where(allow, jnp.exp(sc - top), 0.0)
    total = jnp.sum(prob, axis=1, keepdims=True)
    acc = jnp.dot(prob.astype(jnp.bfloat16), v_ref[...], preferred_element_type=jnp.float32)
    full = acc / total
    o_ref[...] = full.astype(o_ref.dtype)
    part = jnp.sum(full * r_ref[...], axis=1, keepdims=True)

    @pl.when(h == 0)
    def _():
        s_ref[...] = part

    @pl.when(h > 0)
    def _():
        s_ref[...] += part


def attend(q, kall, vall, qpos, qseg, kpos, kseg, readout, interpret=False):
    tok, width = q.shape
    nk, hd = kall.shape
    heads = width // hd
    return pl.pallas_call(
        attend_kernel,
        grid=(heads,),
        in_specs=[
            pl.BlockSpec((tok, hd), lambda h: (0, h)),
            pl.BlockSpec((nk, hd), lambda h: (0, 0)),
            pl.BlockSpec((nk, hd), lambda h: (0, 0)),
            pl.BlockSpec((tok, 1), lambda h: (0, 0)),
            pl.BlockSpec((tok, 1), lambda h: (0, 0)),
            pl.BlockSpec((1, nk), lambda h: (0, 0)),
            pl.BlockSpec((1, nk), lambda h: (0, 0)),
            pl.BlockSpec((1, hd), lambda h: (0, h)),
        ],
        out_specs=[
            pl.BlockSpec((tok, hd), lambda h: (0, h)),
            pl.BlockSpec((tok, 1), lambda h: (0, 0)),
        ],
        out_shape=[
            jax.ShapeDtypeStruct((tok, width), jnp.bfloat16),
            jax.ShapeDtypeStruct((tok, 1), jnp.float32),
        ],
        compiler_params=pltpu.CompilerParams(dimension_semantics=("arbitrary",)),
        interpret=interpret,
    )(q, kall, vall, qpos, qseg, kpos, kseg, readout)


def per_device(queries, keys, values, segment_ids, span_ids, readout):
    tok = queries.shape[1]
    head_dim = keys.shape[2]
    n_ctx = lax.axis_size("ctx")
    back = min((MAX_SEGMENT - 1 + tok - 1) // tok, n_ctx - 1)
    here = lax.axis_index("ctx")
    qseg = segment_ids[0]
    qpos = here * tok + jnp.arange(tok)

    kv = jnp.concatenate([keys[0], values[0]], axis=1)
    segrow = jnp.broadcast_to(qseg.astype(jnp.bfloat16)[None, :], (16, tok))
    segrow = jnp.pad(segrow, ((0, 0), (0, 2 * head_dim - tok))) if tok < 2 * head_dim else segrow[:, : 2 * head_dim]
    packed = jnp.concatenate([kv, segrow], axis=0)
    pieces = []
    for d in range(back, 0, -1):
        pairs = [(i, i + d) for i in range(n_ctx - d)]
        pieces.append(lax.ppermute(packed, "ctx", pairs))
    pieces.append(packed)
    kall = jnp.concatenate([p[:tok, :head_dim] for p in pieces], axis=0)
    vall = jnp.concatenate([p[:tok, head_dim:] for p in pieces], axis=0)
    sall = jnp.concatenate([p[tok, :tok] for p in pieces], axis=0).astype(jnp.float32)
    kpos = (here - back) * tok + jnp.arange((back + 1) * tok, dtype=jnp.int32)

    attended, score = attend(
        queries[0], kall, vall,
        qpos.astype(jnp.int32)[:, None], qseg.astype(jnp.float32)[:, None],
        kpos[None, :], sall[None, :], readout[None, :],
    )
    score = score[:, 0]
    spans = span_ids[0]
    partial_value = (
        jnp.stack(
            [jnp.sum(jnp.where(spans == 1, score, 0.0)), jnp.sum(jnp.where(spans == 2, score, 0.0))]
        )
        / 64.0
    )
    span_scores = lax.psum(lax.all_gather(partial_value, "ctx").sum(0), "phase")
    every = lax.all_gather(span_scores, "dp")
    pair_loss = jnp.mean(jax.nn.softplus(-(every[:, 0] - every[:, 1])))
    return (attended[None], span_scores[None], pair_loss)


def solution(mesh):
    in_specs = (
        P("dp", "ctx", "phase"),
        P("dp", "ctx", "phase"),
        P("dp", "ctx", "phase"),
        P("dp", "ctx"),
        P("dp", "ctx"),
        P("phase"),
    )
    out_specs = (P("dp", "ctx", "phase"), P("dp", None), P())
    return jax.shard_map(
        per_device, mesh=mesh, in_specs=in_specs, out_specs=out_specs, check_vma=False
    )
```

```python
import jax
import jax.numpy as jnp
from jax import lax
from jax.experimental import pallas as pl
from jax.experimental.pallas import tpu as pltpu
from jax.sharding import PartitionSpec as P

MAX_SEGMENT = 1024
MASKED = -1e30


def attend_kernel(here_ref, *refs):
    npieces = len(refs) - 10
    pieces = refs[:npieces]
    q_ref, qseg_ref, span_ref, r_ref, o_ref, part_ref, k_all, v_all, bias, score = refs[npieces:]
    h = pl.program_id(0)
    tok, hd = q_ref.shape

    @pl.when(h == 0)
    def _():
        here = here_ref[0]
        qpos = here * tok + lax.broadcasted_iota(jnp.int32, (tok, 1), 0)
        qseg = qseg_ref[...]
        for i, p_ref in enumerate(pieces):
            k_all[pl.ds(i * tok, tok), :] = p_ref[pl.ds(0, tok), pl.ds(0, hd)]
            v_all[pl.ds(i * tok, tok), :] = p_ref[pl.ds(0, tok), pl.ds(hd, hd)]
            kseg = p_ref[pl.ds(tok, 16), pl.ds(0, tok)].astype(jnp.float32)[0:1, :]
            kpos = (here - (npieces - 1 - i)) * tok + lax.broadcasted_iota(jnp.int32, (1, tok), 1)
            allow = (kpos <= qpos) & (kpos >= 0) & (kseg == qseg)
            bias[:, pl.ds(i * tok, tok)] = jnp.where(allow, 0.0, MASKED)
        score[...] = jnp.zeros_like(score)

    scale = 1.0 / jnp.sqrt(jnp.float32(hd))
    sc = lax.dot_general(
        q_ref[...], k_all[...], (((1,), (1,)), ((), ())), preferred_element_type=jnp.float32
    )
    sc = sc * scale + bias[...]
    top = jnp.max(sc, axis=1, keepdims=True)
    prob = jnp.exp(sc - top)
    total = jnp.sum(prob, axis=1, keepdims=True)
    acc = jnp.dot(prob.astype(jnp.bfloat16), v_all[...], preferred_element_type=jnp.float32)
    full = acc / total
    o_ref[...] = full.astype(o_ref.dtype)
    score[...] += jnp.sum(full * r_ref[...], axis=1, keepdims=True)

    @pl.when(h == pl.num_programs(0) - 1)
    def _():
        spans = span_ref[...]
        s = score[...]
        chosen = jnp.sum(jnp.where(spans == 1, s, 0.0), axis=0, keepdims=True)
        reject = jnp.sum(jnp.where(spans == 2, s, 0.0), axis=0, keepdims=True)
        part_ref[...] = jnp.concatenate([chosen, reject], axis=1) / 64.0


def attend(here, pieces, q, qseg, spans, readout, interpret=False):
    tok, width = q.shape
    hd = pieces[0].shape[1] // 2
    heads = width // hd
    n = len(pieces)
    full = lambda shape: pl.BlockSpec(shape, lambda h, here: (0, 0))
    grid_spec = pltpu.PrefetchScalarGridSpec(
        num_scalar_prefetch=1,
        grid=(heads,),
        in_specs=[full(p.shape) for p in pieces]
        + [
            pl.BlockSpec((tok, hd), lambda h, here: (0, h)),
            full((tok, 1)),
            full((tok, 1)),
            pl.BlockSpec((1, hd), lambda h, here: (0, h)),
        ],
        out_specs=[pl.BlockSpec((tok, hd), lambda h, here: (0, h)), full((1, 2))],
        scratch_shapes=[
            pltpu.VMEM((n * tok, hd), jnp.bfloat16),
            pltpu.VMEM((n * tok, hd), jnp.bfloat16),
            pltpu.VMEM((tok, n * tok), jnp.float32),
            pltpu.VMEM((tok, 1), jnp.float32),
        ],
    )
    return pl.pallas_call(
        attend_kernel,
        grid_spec=grid_spec,
        out_shape=[
            jax.ShapeDtypeStruct((tok, width), jnp.bfloat16),
            jax.ShapeDtypeStruct((1, 2), jnp.float32),
        ],
        compiler_params=pltpu.CompilerParams(dimension_semantics=("arbitrary",)),
        interpret=interpret,
    )(here, *pieces, q, qseg, spans, readout)


def per_device(queries, keys, values, segment_ids, span_ids, readout):
    tok = queries.shape[1]
    head_dim = keys.shape[2]
    n_ctx = lax.axis_size("ctx")
    back = min((MAX_SEGMENT - 1 + tok - 1) // tok, n_ctx - 1)
    here = lax.axis_index("ctx")
    qseg = segment_ids[0]

    kv = jnp.concatenate([keys[0], values[0]], axis=1)
    segrow = jnp.broadcast_to(qseg.astype(jnp.bfloat16)[None, :], (16, tok))
    segrow = jnp.pad(segrow, ((0, 0), (0, 2 * head_dim - tok))) if tok < 2 * head_dim else segrow[:, : 2 * head_dim]
    packed = jnp.concatenate([kv, segrow], axis=0)
    pieces = []
    for d in range(back, 0, -1):
        pairs = [(i, i + d) for i in range(n_ctx - d)]
        pieces.append(lax.ppermute(packed, "ctx", pairs))
    pieces.append(packed)

    attended, part = attend(
        jnp.reshape(here, (1,)).astype(jnp.int32), pieces, queries[0],
        qseg.astype(jnp.float32)[:, None], span_ids[0][:, None], readout[None, :],
    )
    span_scores = lax.psum(lax.all_gather(part[0], "ctx").sum(0), "phase")
    every = lax.all_gather(span_scores, "dp")
    pair_loss = jnp.mean(jax.nn.softplus(-(every[:, 0] - every[:, 1])))
    return (attended[None], span_scores[None], pair_loss)


def solution(mesh):
    in_specs = (
        P("dp", "ctx", "phase"),
        P("dp", "ctx", "phase"),
        P("dp", "ctx", "phase"),
        P("dp", "ctx"),
        P("dp", "ctx"),
        P("phase"),
    )
    out_specs = (P("dp", "ctx", "phase"), P("dp", None), P())
    return jax.shard_map(
        per_device, mesh=mesh, in_specs=in_specs, out_specs=out_specs, check_vma=False
    )
```

```python
import jax
import jax.numpy as jnp
from jax import lax
from jax.experimental import pallas as pl
from jax.experimental.pallas import tpu as pltpu
from jax.sharding import PartitionSpec as P

MAX_SEGMENT = 1024
MASKED = -1e30


def attend_kernel(here_ref, *refs):
    npieces = len(refs) - 10
    pieces = refs[:npieces]
    q_ref, qseg_ref, span_ref, r_ref, o_ref, part_ref, k_all, v_all, bias, score = refs[npieces:]
    h = pl.program_id(0)
    tok, hd = q_ref.shape

    @pl.when(h == 0)
    def _():
        here = here_ref[0]
        qpos = here * tok + lax.broadcasted_iota(jnp.int32, (tok, 1), 0)
        qseg = qseg_ref[...]
        for i, p_ref in enumerate(pieces):
            k_all[pl.ds(i * tok, tok), :] = p_ref[pl.ds(0, tok), pl.ds(0, hd)]
            v_all[pl.ds(i * tok, tok), :] = p_ref[pl.ds(0, tok), pl.ds(hd, hd)]
            kseg = p_ref[pl.ds(tok, 16), pl.ds(0, tok)].astype(jnp.float32)[0:1, :]
            kpos = (here - (npieces - 1 - i)) * tok + lax.broadcasted_iota(jnp.int32, (1, tok), 1)
            allow = (kpos <= qpos) & (kpos >= 0) & (kseg == qseg)
            bias[:, pl.ds(i * tok, tok)] = jnp.where(allow, 0.0, MASKED)
        score[...] = jnp.zeros_like(score)

    scale = 1.0 / jnp.sqrt(jnp.float32(hd))
    sc = lax.dot_general(
        q_ref[...], k_all[...], (((1,), (1,)), ((), ())), preferred_element_type=jnp.float32
    )
    sc = sc * scale + bias[...]
    top = jnp.max(sc, axis=1, keepdims=True)
    prob = jnp.exp(sc - top)
    total = jnp.sum(prob, axis=1, keepdims=True)
    acc = jnp.dot(prob.astype(jnp.bfloat16), v_all[...], preferred_element_type=jnp.float32)
    full = acc / total
    o_ref[...] = full.astype(o_ref.dtype)
    score[...] += jnp.sum(full * r_ref[...], axis=1, keepdims=True)

    @pl.when(h == pl.num_programs(0) - 1)
    def _():
        spans = span_ref[...]
        s = score[...]
        chosen = jnp.sum(jnp.where(spans == 1, s, 0.0), axis=0, keepdims=True)
        reject = jnp.sum(jnp.where(spans == 2, s, 0.0), axis=0, keepdims=True)
        part_ref[...] = jnp.concatenate([chosen, reject], axis=1) / 64.0


def attend(here, pieces, q, qseg, spans, readout, interpret=False):
    tok, width = q.shape
    hd = pieces[0].shape[1] // 2
    heads = width // hd
    n = len(pieces)
    full = lambda shape: pl.BlockSpec(shape, lambda h, here: (0, 0))
    grid_spec = pltpu.PrefetchScalarGridSpec(
        num_scalar_prefetch=1,
        grid=(heads,),
        in_specs=[full(p.shape) for p in pieces]
        + [
            pl.BlockSpec((tok, hd), lambda h, here: (0, h)),
            full((tok, 1)),
            full((tok, 1)),
            pl.BlockSpec((1, hd), lambda h, here: (0, h)),
        ],
        out_specs=[pl.BlockSpec((tok, hd), lambda h, here: (0, h)), full((1, 2))],
        scratch_shapes=[
            pltpu.VMEM((n * tok, hd), jnp.bfloat16),
            pltpu.VMEM((n * tok, hd), jnp.bfloat16),
            pltpu.VMEM((tok, n * tok), jnp.float32),
            pltpu.VMEM((tok, 1), jnp.float32),
        ],
    )
    return pl.pallas_call(
        attend_kernel,
        grid_spec=grid_spec,
        out_shape=[
            jax.ShapeDtypeStruct((tok, width), jnp.bfloat16),
            jax.ShapeDtypeStruct((1, 2), jnp.float32),
        ],
        compiler_params=pltpu.CompilerParams(dimension_semantics=("arbitrary",)),
        interpret=interpret,
    )(here, *pieces, q, qseg, spans, readout)


def gathered(value, axes):
    count = lax.axis_size(axes)
    copies = jnp.broadcast_to(value[None], (count,) + value.shape)
    return lax.all_to_all(copies, axes, 0, 0, tiled=False)


def per_device(queries, keys, values, segment_ids, span_ids, readout):
    tok = queries.shape[1]
    head_dim = keys.shape[2]
    n_ctx = lax.axis_size("ctx")
    back = min((MAX_SEGMENT - 1 + tok - 1) // tok, n_ctx - 1)
    here = lax.axis_index("ctx")
    qseg = segment_ids[0]

    kv = jnp.concatenate([keys[0], values[0]], axis=1)
    segrow = jnp.broadcast_to(qseg.astype(jnp.bfloat16)[None, :], (16, tok))
    segrow = jnp.pad(segrow, ((0, 0), (0, 2 * head_dim - tok))) if tok < 2 * head_dim else segrow[:, : 2 * head_dim]
    packed = jnp.concatenate([kv, segrow], axis=0)
    pieces = []
    for d in range(back, 0, -1):
        pairs = [(i, i + d) for i in range(n_ctx - d)]
        pieces.append(lax.ppermute(packed, "ctx", pairs))
    pieces.append(packed)

    attended, part = attend(
        jnp.reshape(here, (1,)).astype(jnp.int32), pieces, queries[0],
        qseg.astype(jnp.float32)[:, None], span_ids[0][:, None], readout[None, :],
    )
    span_scores = gathered(part[0], ("phase", "ctx")).sum(0)
    every = gathered(span_scores, "dp")
    pair_loss = jnp.mean(jax.nn.softplus(-(every[:, 0] - every[:, 1])))
    return (attended[None], span_scores[None], pair_loss)


def solution(mesh):
    in_specs = (
        P("dp", "ctx", "phase"),
        P("dp", "ctx", "phase"),
        P("dp", "ctx", "phase"),
        P("dp", "ctx"),
        P("dp", "ctx"),
        P("phase"),
    )
    out_specs = (P("dp", "ctx", "phase"), P("dp", None), P())
    return jax.shard_map(
        per_device, mesh=mesh, in_specs=in_specs, out_specs=out_specs, check_vma=False
    )
```

```python
import jax
import jax.numpy as jnp
from jax import lax
from jax.experimental import pallas as pl
from jax.experimental.pallas import tpu as pltpu
from jax.sharding import PartitionSpec as P

MAX_SEGMENT = 1024
MASKED = -1e30


def attend_kernel(here_ref, *refs):
    npieces = len(refs) - 8
    pieces = refs[:npieces]
    q_ref, qseg_ref, span_ref, r_ref, o_ref, part_ref, k_all, v_all = refs[npieces:]
    tok, width = q_ref.shape
    hd = k_all.shape[1]
    here = here_ref[0]
    qpos = here * tok + lax.broadcasted_iota(jnp.int32, (tok, 1), 0)
    qseg = qseg_ref[...]
    biases = []
    for i, p_ref in enumerate(pieces):
        k_all[pl.ds(i * tok, tok), :] = p_ref[pl.ds(0, tok), pl.ds(0, hd)]
        v_all[pl.ds(i * tok, tok), :] = p_ref[pl.ds(0, tok), pl.ds(hd, hd)]
        kseg = p_ref[pl.ds(tok, 16), pl.ds(0, tok)].astype(jnp.float32)[0:1, :]
        kpos = (here - (npieces - 1 - i)) * tok + lax.broadcasted_iota(jnp.int32, (1, tok), 1)
        allow = (kpos <= qpos) & (kpos >= 0) & (kseg == qseg)
        biases.append(jnp.where(allow, 0.0, MASKED))
    bias = jnp.concatenate(biases, axis=1)
    scale = 1.0 / jnp.sqrt(jnp.float32(hd))
    score = jnp.zeros((tok, 1), jnp.float32)
    for h in range(width // hd):
        cols = pl.ds(h * hd, hd)
        sc = lax.dot_general(
            q_ref[:, cols], k_all[...], (((1,), (1,)), ((), ())), preferred_element_type=jnp.float32
        )
        sc = sc * scale + bias
        top = jnp.max(sc, axis=1, keepdims=True)
        prob = jnp.exp(sc - top)
        total = jnp.sum(prob, axis=1, keepdims=True)
        acc = jnp.dot(prob.astype(jnp.bfloat16), v_all[...], preferred_element_type=jnp.float32)
        full = acc / total
        o_ref[:, cols] = full.astype(o_ref.dtype)
        score = score + jnp.sum(full * r_ref[:, cols], axis=1, keepdims=True)
    spans = span_ref[...]
    chosen = jnp.sum(jnp.where(spans == 1, score, 0.0), axis=0, keepdims=True)
    reject = jnp.sum(jnp.where(spans == 2, score, 0.0), axis=0, keepdims=True)
    part_ref[...] = jnp.concatenate([chosen, reject], axis=1) / 64.0


def attend(here, pieces, q, qseg, spans, readout, interpret=False):
    tok, width = q.shape
    hd = pieces[0].shape[1] // 2
    n = len(pieces)
    full = lambda shape: pl.BlockSpec(shape, lambda h, here: (0, 0))
    grid_spec = pltpu.PrefetchScalarGridSpec(
        num_scalar_prefetch=1,
        grid=(1,),
        in_specs=[full(p.shape) for p in pieces]
        + [full((tok, width)), full((tok, 1)), full((tok, 1)), full((1, width))],
        out_specs=[full((tok, width)), full((1, 2))],
        scratch_shapes=[
            pltpu.VMEM((n * tok, hd), jnp.bfloat16),
            pltpu.VMEM((n * tok, hd), jnp.bfloat16),
        ],
    )
    return pl.pallas_call(
        attend_kernel,
        grid_spec=grid_spec,
        out_shape=[
            jax.ShapeDtypeStruct((tok, width), jnp.bfloat16),
            jax.ShapeDtypeStruct((1, 2), jnp.float32),
        ],
        compiler_params=pltpu.CompilerParams(dimension_semantics=("arbitrary",)),
        interpret=interpret,
    )(here, *pieces, q, qseg, spans, readout)


def gathered(value, axes):
    count = lax.axis_size(axes)
    copies = jnp.broadcast_to(value[None], (count,) + value.shape)
    return lax.all_to_all(copies, axes, 0, 0, tiled=False)


def per_device(queries, keys, values, segment_ids, span_ids, readout):
    tok = queries.shape[1]
    head_dim = keys.shape[2]
    n_ctx = lax.axis_size("ctx")
    back = min((MAX_SEGMENT - 1 + tok - 1) // tok, n_ctx - 1)
    here = lax.axis_index("ctx")
    qseg = segment_ids[0]

    kv = jnp.concatenate([keys[0], values[0]], axis=1)
    segrow = jnp.broadcast_to(qseg.astype(jnp.bfloat16)[None, :], (16, tok))
    segrow = jnp.pad(segrow, ((0, 0), (0, 2 * head_dim - tok))) if tok < 2 * head_dim else segrow[:, : 2 * head_dim]
    packed = jnp.concatenate([kv, segrow], axis=0)
    pieces = []
    for d in range(back, 0, -1):
        pairs = [(i, i + d) for i in range(n_ctx - d)]
        pieces.append(lax.ppermute(packed, "ctx", pairs))
    pieces.append(packed)

    attended, part = attend(
        jnp.reshape(here, (1,)).astype(jnp.int32), pieces, queries[0],
        qseg.astype(jnp.float32)[:, None], span_ids[0][:, None], readout[None, :],
    )
    span_scores = gathered(part[0], ("phase", "ctx")).sum(0)
    every = gathered(span_scores, "dp")
    pair_loss = jnp.mean(jax.nn.softplus(-(every[:, 0] - every[:, 1])))
    return (attended[None], span_scores[None], pair_loss)


def solution(mesh):
    in_specs = (
        P("dp", "ctx", "phase"),
        P("dp", "ctx", "phase"),
        P("dp", "ctx", "phase"),
        P("dp", "ctx"),
        P("dp", "ctx"),
        P("phase"),
    )
    out_specs = (P("dp", "ctx", "phase"), P("dp", None), P())
    return jax.shard_map(
        per_device, mesh=mesh, in_specs=in_specs, out_specs=out_specs, check_vma=False
    )
```

```python
import jax
import jax.numpy as jnp
from jax import lax
from jax.experimental import pallas as pl
from jax.experimental.pallas import tpu as pltpu
from jax.sharding import PartitionSpec as P

MAX_SEGMENT = 1024
MASKED = -1e30


def attend_kernel(here_ref, *refs):
    npieces = len(refs) - 6
    pieces = refs[:npieces]
    q_ref, r_ref, o_ref, part_ref, k_all, v_all = refs[npieces:]
    tok, width = q_ref.shape
    hd = k_all.shape[1]
    here = here_ref[0]
    qpos = here * tok + lax.broadcasted_iota(jnp.int32, (tok, 1), 0)
    rows = pieces[-1][pl.ds(tok, 16), pl.ds(0, tok)].astype(jnp.float32)
    half = 64
    both = jnp.concatenate(
        [jnp.broadcast_to(rows[0:1], (half, tok)), jnp.broadcast_to(rows[1:2], (half, tok))], axis=0
    )
    cols = jnp.transpose(both)
    qseg = cols[:, 0:1]
    spans = cols[:, half : half + 1]
    biases = []
    for i, p_ref in enumerate(pieces):
        k_all[pl.ds(i * tok, tok), :] = p_ref[pl.ds(0, tok), pl.ds(0, hd)]
        v_all[pl.ds(i * tok, tok), :] = p_ref[pl.ds(0, tok), pl.ds(hd, hd)]
        kseg = p_ref[pl.ds(tok, 16), pl.ds(0, tok)].astype(jnp.float32)[0:1, :]
        kpos = (here - (npieces - 1 - i)) * tok + lax.broadcasted_iota(jnp.int32, (1, tok), 1)
        allow = (kpos <= qpos) & (kpos >= 0) & (kseg == qseg)
        biases.append(jnp.where(allow, 0.0, MASKED))
    bias = jnp.concatenate(biases, axis=1)
    scale = 1.0 / jnp.sqrt(jnp.float32(hd))
    score = jnp.zeros((tok, 1), jnp.float32)
    for h in range(width // hd):
        cols = pl.ds(h * hd, hd)
        sc = lax.dot_general(
            q_ref[:, cols], k_all[...], (((1,), (1,)), ((), ())), preferred_element_type=jnp.float32
        )
        sc = sc * scale + bias
        top = jnp.max(sc, axis=1, keepdims=True)
        prob = jnp.exp(sc - top)
        total = jnp.sum(prob, axis=1, keepdims=True)
        acc = jnp.dot(prob.astype(jnp.bfloat16), v_all[...], preferred_element_type=jnp.float32)
        full = acc / total
        o_ref[:, cols] = full.astype(o_ref.dtype)
        score = score + jnp.sum(full * r_ref[:, cols], axis=1, keepdims=True)
    chosen = jnp.sum(jnp.where(spans == 1, score, 0.0), axis=0, keepdims=True)
    reject = jnp.sum(jnp.where(spans == 2, score, 0.0), axis=0, keepdims=True)
    part_ref[...] = jnp.concatenate([chosen, reject], axis=1) / 64.0


def attend(here, pieces, q, readout, interpret=False):
    tok, width = q.shape
    hd = pieces[0].shape[1] // 2
    n = len(pieces)
    full = lambda shape: pl.BlockSpec(shape, lambda h, here: (0, 0))
    grid_spec = pltpu.PrefetchScalarGridSpec(
        num_scalar_prefetch=1,
        grid=(1,),
        in_specs=[full(p.shape) for p in pieces]
        + [full((tok, width)), full((1, width))],
        out_specs=[full((tok, width)), full((1, 2))],
        scratch_shapes=[
            pltpu.VMEM((n * tok, hd), jnp.bfloat16),
            pltpu.VMEM((n * tok, hd), jnp.bfloat16),
        ],
    )
    return pl.pallas_call(
        attend_kernel,
        grid_spec=grid_spec,
        out_shape=[
            jax.ShapeDtypeStruct((tok, width), jnp.bfloat16),
            jax.ShapeDtypeStruct((1, 2), jnp.float32),
        ],
        compiler_params=pltpu.CompilerParams(dimension_semantics=("arbitrary",)),
        interpret=interpret,
    )(here, *pieces, q, readout)


def gathered(value, axes):
    count = lax.axis_size(axes)
    copies = jnp.broadcast_to(value[None], (count,) + value.shape)
    return lax.all_to_all(copies, axes, 0, 0, tiled=False)


def per_device(queries, keys, values, segment_ids, span_ids, readout):
    tok = queries.shape[1]
    head_dim = keys.shape[2]
    n_ctx = lax.axis_size("ctx")
    back = min((MAX_SEGMENT - 1 + tok - 1) // tok, n_ctx - 1)
    here = lax.axis_index("ctx")
    qseg = segment_ids[0]

    kv = jnp.concatenate([keys[0], values[0]], axis=1)
    ids = jnp.stack([qseg, span_ids[0]]).astype(jnp.bfloat16)
    segrow = jnp.concatenate([ids, jnp.zeros((14, tok), jnp.bfloat16)], axis=0)
    segrow = jnp.pad(segrow, ((0, 0), (0, 2 * head_dim - tok))) if tok < 2 * head_dim else segrow[:, : 2 * head_dim]
    packed = jnp.concatenate([kv, segrow], axis=0)
    pieces = []
    for d in range(back, 0, -1):
        pairs = [(i, i + d) for i in range(n_ctx - d)]
        pieces.append(lax.ppermute(packed, "ctx", pairs))
    pieces.append(packed)

    attended, part = attend(
        jnp.reshape(here, (1,)).astype(jnp.int32), pieces, queries[0], readout[None, :]
    )
    span_scores = gathered(part[0], ("phase", "ctx")).sum(0)
    every = gathered(span_scores, "dp")
    pair_loss = jnp.mean(jax.nn.softplus(-(every[:, 0] - every[:, 1])))
    return (attended[None], span_scores[None], pair_loss)


def solution(mesh):
    in_specs = (
        P("dp", "ctx", "phase"),
        P("dp", "ctx", "phase"),
        P("dp", "ctx", "phase"),
        P("dp", "ctx"),
        P("dp", "ctx"),
        P("phase"),
    )
    out_specs = (P("dp", "ctx", "phase"), P("dp", None), P())
    return jax.shard_map(
        per_device, mesh=mesh, in_specs=in_specs, out_specs=out_specs, check_vma=False
    )
```

```python
import jax
import jax.numpy as jnp
from jax import lax
from jax.experimental import pallas as pl
from jax.experimental.pallas import tpu as pltpu
from jax.sharding import PartitionSpec as P

MAX_SEGMENT = 1024
MASKED = -1e30


def attend_kernel(here_ref, *refs):
    npieces = len(refs) - 6
    pieces = refs[:npieces]
    q_ref, r_ref, o_ref, part_ref, k_all, v_all = refs[npieces:]
    tok, width = q_ref.shape
    hd = k_all.shape[1]
    here = here_ref[0]
    qpos = here * tok + lax.broadcasted_iota(jnp.int32, (tok, 1), 0)
    rows = pieces[-1][pl.ds(tok, 16), pl.ds(0, tok)].astype(jnp.float32)
    half = 64
    both = jnp.concatenate(
        [jnp.broadcast_to(rows[0:1], (half, tok)), jnp.broadcast_to(rows[1:2], (half, tok))], axis=0
    )
    cols = jnp.transpose(both)
    qseg = cols[:, 0:1]
    spans = cols[:, half : half + 1]
    biases = []
    for i, p_ref in enumerate(pieces):
        k_all[pl.ds(i * tok, tok), :] = p_ref[pl.ds(0, tok), pl.ds(0, hd)]
        v_all[pl.ds(i * tok, tok), :] = p_ref[pl.ds(0, tok), pl.ds(hd, hd)]
        kseg = p_ref[pl.ds(tok, 16), pl.ds(0, tok)].astype(jnp.float32)[0:1, :]
        back = npieces - 1 - i
        if back == 0:
            kpos = here * tok + lax.broadcasted_iota(jnp.int32, (1, tok), 1)
            allow = (kpos <= qpos) & (kseg == qseg)
        else:
            allow = (kseg == qseg) & (here >= back)
        biases.append(jnp.where(allow, 0.0, MASKED))
    bias = jnp.concatenate(biases, axis=1)
    scale = 1.0 / jnp.sqrt(jnp.float32(hd))
    score = jnp.zeros((tok, 1), jnp.float32)
    for h in range(width // hd):
        cols = pl.ds(h * hd, hd)
        sc = lax.dot_general(
            q_ref[:, cols], k_all[...], (((1,), (1,)), ((), ())), preferred_element_type=jnp.float32
        )
        sc = sc * scale + bias
        top = jnp.max(sc, axis=1, keepdims=True)
        prob = jnp.exp(sc - top)
        total = jnp.sum(prob, axis=1, keepdims=True)
        acc = jnp.dot(prob.astype(jnp.bfloat16), v_all[...], preferred_element_type=jnp.float32)
        full = acc / total
        o_ref[:, cols] = full.astype(o_ref.dtype)
        score = score + jnp.sum(full * r_ref[:, cols], axis=1, keepdims=True)
    chosen = jnp.sum(jnp.where(spans == 1, score, 0.0), axis=0, keepdims=True)
    reject = jnp.sum(jnp.where(spans == 2, score, 0.0), axis=0, keepdims=True)
    part_ref[...] = jnp.concatenate([chosen, reject], axis=1) / 64.0


def attend(here, pieces, q, readout, interpret=False):
    tok, width = q.shape
    hd = pieces[0].shape[1] // 2
    n = len(pieces)
    full = lambda shape: pl.BlockSpec(shape, lambda h, here: (0, 0))
    grid_spec = pltpu.PrefetchScalarGridSpec(
        num_scalar_prefetch=1,
        grid=(1,),
        in_specs=[full(p.shape) for p in pieces]
        + [full((tok, width)), full((1, width))],
        out_specs=[full((tok, width)), full((1, 2))],
        scratch_shapes=[
            pltpu.VMEM((n * tok, hd), jnp.bfloat16),
            pltpu.VMEM((n * tok, hd), jnp.bfloat16),
        ],
    )
    return pl.pallas_call(
        attend_kernel,
        grid_spec=grid_spec,
        out_shape=[
            jax.ShapeDtypeStruct((tok, width), jnp.bfloat16),
            jax.ShapeDtypeStruct((1, 2), jnp.float32),
        ],
        compiler_params=pltpu.CompilerParams(dimension_semantics=("arbitrary",)),
        interpret=interpret,
    )(here, *pieces, q, readout)


def gathered(value, axes):
    count = lax.axis_size(axes)
    copies = jnp.broadcast_to(value[None], (count,) + value.shape)
    return lax.all_to_all(copies, axes, 0, 0, tiled=False)


def per_device(queries, keys, values, segment_ids, span_ids, readout):
    tok = queries.shape[1]
    head_dim = keys.shape[2]
    n_ctx = lax.axis_size("ctx")
    back = min((MAX_SEGMENT - 1 + tok - 1) // tok, n_ctx - 1)
    here = lax.axis_index("ctx")
    qseg = segment_ids[0]

    kv = jnp.concatenate([keys[0], values[0]], axis=1)
    ids = jnp.stack([qseg, span_ids[0]]).astype(jnp.bfloat16)
    segrow = jnp.concatenate([ids, jnp.zeros((14, tok), jnp.bfloat16)], axis=0)
    segrow = jnp.pad(segrow, ((0, 0), (0, 2 * head_dim - tok))) if tok < 2 * head_dim else segrow[:, : 2 * head_dim]
    packed = jnp.concatenate([kv, segrow], axis=0)
    pieces = []
    for d in range(back, 0, -1):
        pairs = [(i, i + d) for i in range(n_ctx - d)]
        pieces.append(lax.ppermute(packed, "ctx", pairs))
    pieces.append(packed)

    attended, part = attend(
        jnp.reshape(here, (1,)).astype(jnp.int32), pieces, queries[0], readout[None, :]
    )
    span_scores = gathered(part[0], ("phase", "ctx")).sum(0)
    every = gathered(span_scores, "dp")
    pair_loss = jnp.mean(jax.nn.softplus(-(every[:, 0] - every[:, 1])))
    return (attended[None], span_scores[None], pair_loss)


def solution(mesh):
    in_specs = (
        P("dp", "ctx", "phase"),
        P("dp", "ctx", "phase"),
        P("dp", "ctx", "phase"),
        P("dp", "ctx"),
        P("dp", "ctx"),
        P("phase"),
    )
    out_specs = (P("dp", "ctx", "phase"), P("dp", None), P())
    return jax.shard_map(
        per_device, mesh=mesh, in_specs=in_specs, out_specs=out_specs, check_vma=False
    )
```

```python
import jax
import jax.numpy as jnp
from jax import lax
from jax.experimental import pallas as pl
from jax.experimental.pallas import tpu as pltpu
from jax.sharding import PartitionSpec as P

MAX_SEGMENT = 1024
MASKED = -1e30


def attend_kernel(here_ref, *refs):
    npieces = len(refs) - 4
    pieces = refs[:npieces]
    q_ref, r_ref, o_ref, part_ref = refs[npieces:]
    tok, width = q_ref.shape
    hd = pieces[0].shape[1] // 2
    here = here_ref[0]
    qpos = here * tok + lax.broadcasted_iota(jnp.int32, (tok, 1), 0)
    rows = pieces[-1][pl.ds(tok, 16), pl.ds(0, tok)].astype(jnp.float32)
    half = 64
    both = jnp.concatenate(
        [jnp.broadcast_to(rows[0:1], (half, tok)), jnp.broadcast_to(rows[1:2], (half, tok))], axis=0
    )
    cols = jnp.transpose(both)
    qseg = cols[:, 0:1]
    spans = cols[:, half : half + 1]
    biases = []
    for i, p_ref in enumerate(pieces):
        kseg = p_ref[pl.ds(tok, 16), pl.ds(0, tok)].astype(jnp.float32)[0:1, :]
        kpos = (here - (npieces - 1 - i)) * tok + lax.broadcasted_iota(jnp.int32, (1, tok), 1)
        allow = (kpos <= qpos) & (kpos >= 0) & (kseg == qseg)
        biases.append(jnp.where(allow, 0.0, MASKED))
    scale = 1.0 / jnp.sqrt(jnp.float32(hd))
    score = jnp.zeros((tok, 1), jnp.float32)
    for h in range(width // hd):
        cols = pl.ds(h * hd, hd)
        qh = q_ref[:, cols]
        scs = []
        for i, p_ref in enumerate(pieces):
            sc = lax.dot_general(
                qh, p_ref[pl.ds(0, tok), pl.ds(0, hd)], (((1,), (1,)), ((), ())),
                preferred_element_type=jnp.float32,
            )
            scs.append(sc * scale + biases[i])
        top = scs[0].max(axis=1, keepdims=True)
        for sc in scs[1:]:
            top = jnp.maximum(top, sc.max(axis=1, keepdims=True))
        total = jnp.zeros((tok, 1), jnp.float32)
        acc = jnp.zeros((tok, hd), jnp.float32)
        for i, p_ref in enumerate(pieces):
            prob = jnp.exp(scs[i] - top)
            total = total + jnp.sum(prob, axis=1, keepdims=True)
            acc = acc + jnp.dot(
                prob.astype(jnp.bfloat16), p_ref[pl.ds(0, tok), pl.ds(hd, hd)],
                preferred_element_type=jnp.float32,
            )
        full = acc / total
        o_ref[:, cols] = full.astype(o_ref.dtype)
        score = score + jnp.sum(full * r_ref[:, cols], axis=1, keepdims=True)
    chosen = jnp.sum(jnp.where(spans == 1, score, 0.0), axis=0, keepdims=True)
    reject = jnp.sum(jnp.where(spans == 2, score, 0.0), axis=0, keepdims=True)
    part_ref[...] = jnp.concatenate([chosen, reject], axis=1) / 64.0


def attend(here, pieces, q, readout, interpret=False):
    tok, width = q.shape
    hd = pieces[0].shape[1] // 2
    n = len(pieces)
    full = lambda shape: pl.BlockSpec(shape, lambda h, here: (0, 0))
    grid_spec = pltpu.PrefetchScalarGridSpec(
        num_scalar_prefetch=1,
        grid=(1,),
        in_specs=[full(p.shape) for p in pieces]
        + [full((tok, width)), full((1, width))],
        out_specs=[full((tok, width)), full((1, 2))],
    )
    return pl.pallas_call(
        attend_kernel,
        grid_spec=grid_spec,
        out_shape=[
            jax.ShapeDtypeStruct((tok, width), jnp.bfloat16),
            jax.ShapeDtypeStruct((1, 2), jnp.float32),
        ],
        compiler_params=pltpu.CompilerParams(dimension_semantics=("arbitrary",)),
        interpret=interpret,
    )(here, *pieces, q, readout)


def gathered(value, axes):
    count = lax.axis_size(axes)
    copies = jnp.broadcast_to(value[None], (count,) + value.shape)
    return lax.all_to_all(copies, axes, 0, 0, tiled=False)


def per_device(queries, keys, values, segment_ids, span_ids, readout):
    tok = queries.shape[1]
    head_dim = keys.shape[2]
    n_ctx = lax.axis_size("ctx")
    back = min((MAX_SEGMENT - 1 + tok - 1) // tok, n_ctx - 1)
    here = lax.axis_index("ctx")
    qseg = segment_ids[0]

    kv = jnp.concatenate([keys[0], values[0]], axis=1)
    ids = jnp.stack([qseg, span_ids[0]]).astype(jnp.bfloat16)
    segrow = jnp.concatenate([ids, jnp.zeros((14, tok), jnp.bfloat16)], axis=0)
    segrow = jnp.pad(segrow, ((0, 0), (0, 2 * head_dim - tok))) if tok < 2 * head_dim else segrow[:, : 2 * head_dim]
    packed = jnp.concatenate([kv, segrow], axis=0)
    pieces = []
    for d in range(back, 0, -1):
        pairs = [(i, i + d) for i in range(n_ctx - d)]
        pieces.append(lax.ppermute(packed, "ctx", pairs))
    pieces.append(packed)

    attended, part = attend(
        jnp.reshape(here, (1,)).astype(jnp.int32), pieces, queries[0], readout[None, :]
    )
    span_scores = gathered(part[0], ("phase", "ctx")).sum(0)
    every = gathered(span_scores, "dp")
    pair_loss = jnp.mean(jax.nn.softplus(-(every[:, 0] - every[:, 1])))
    return (attended[None], span_scores[None], pair_loss)


def solution(mesh):
    in_specs = (
        P("dp", "ctx", "phase"),
        P("dp", "ctx", "phase"),
        P("dp", "ctx", "phase"),
        P("dp", "ctx"),
        P("dp", "ctx"),
        P("phase"),
    )
    out_specs = (P("dp", "ctx", "phase"), P("dp", None), P())
    return jax.shard_map(
        per_device, mesh=mesh, in_specs=in_specs, out_specs=out_specs, check_vma=False
    )
```

```python
import jax
import jax.numpy as jnp
from jax import lax
from jax.experimental import pallas as pl
from jax.experimental.pallas import tpu as pltpu
from jax.sharding import PartitionSpec as P

MAX_SEGMENT = 1024
MASKED = -1e30


def attend_kernel(here_ref, *refs):
    npieces = len(refs) - 4
    pieces = refs[:npieces]
    q_ref, r_ref, o_ref, part_ref = refs[npieces:]
    tok, width = q_ref.shape
    hd = pieces[0].shape[1] // 2
    here = here_ref[0]
    qpos = here * tok + lax.broadcasted_iota(jnp.int32, (tok, 1), 0)
    rows = pieces[-1][pl.ds(tok, 16), pl.ds(0, tok)].astype(jnp.float32)
    half = 64
    both = jnp.concatenate(
        [jnp.broadcast_to(rows[0:1], (half, tok)), jnp.broadcast_to(rows[1:2], (half, tok))], axis=0
    )
    cols = jnp.transpose(both)
    qseg = cols[:, 0:1]
    spans = cols[:, half : half + 1]
    biases = []
    for i, p_ref in enumerate(pieces):
        kseg = p_ref[pl.ds(tok, 16), pl.ds(0, tok)].astype(jnp.float32)[0:1, :]
        kpos = (here - (npieces - 1 - i)) * tok + lax.broadcasted_iota(jnp.int32, (1, tok), 1)
        allow = (kpos <= qpos) & (kpos >= 0) & (kseg == qseg)
        biases.append(jnp.where(allow, 0.0, MASKED))
    scale = 1.0 / jnp.sqrt(jnp.float32(hd))
    merge = npieces > 1 and (npieces - 1) * tok >= MAX_SEGMENT
    if merge:
        tri = lax.broadcasted_iota(jnp.int32, (tok, tok), 1) <= lax.broadcasted_iota(jnp.int32, (tok, tok), 0)
        chunk_bias = [jnp.where(tri, biases[-1], biases[0])] + biases[1:-1]
    else:
        chunk_bias = biases
    score = jnp.zeros((tok, 1), jnp.float32)
    for h in range(width // hd):
        cols = pl.ds(h * hd, hd)
        qh = q_ref[:, cols]
        raw = [
            lax.dot_general(
                qh, p_ref[pl.ds(0, tok), pl.ds(0, hd)], (((1,), (1,)), ((), ())),
                preferred_element_type=jnp.float32,
            )
            for p_ref in pieces
        ]
        if merge:
            raw = [jnp.where(tri, raw[-1], raw[0])] + raw[1:-1]
        scs = [r * scale + b for r, b in zip(raw, chunk_bias)]
        top = scs[0].max(axis=1, keepdims=True)
        for sc in scs[1:]:
            top = jnp.maximum(top, sc.max(axis=1, keepdims=True))
        total = jnp.zeros((tok, 1), jnp.float32)
        acc = jnp.zeros((tok, hd), jnp.float32)
        for i, sc in enumerate(scs):
            prob = jnp.exp(sc - top)
            total = total + jnp.sum(prob, axis=1, keepdims=True)
            if merge and i == 0:
                own = jnp.where(tri, prob, 0.0)
                acc = acc + jnp.dot(
                    own.astype(jnp.bfloat16), pieces[-1][pl.ds(0, tok), pl.ds(hd, hd)],
                    preferred_element_type=jnp.float32,
                )
                prob = prob - own
                src_ref = pieces[0]
            else:
                src_ref = pieces[i] if not merge else pieces[i]
            acc = acc + jnp.dot(
                prob.astype(jnp.bfloat16), src_ref[pl.ds(0, tok), pl.ds(hd, hd)],
                preferred_element_type=jnp.float32,
            )
        full = acc / total
        o_ref[:, cols] = full.astype(o_ref.dtype)
        score = score + jnp.sum(full * r_ref[:, cols], axis=1, keepdims=True)
    chosen = jnp.sum(jnp.where(spans == 1, score, 0.0), axis=0, keepdims=True)
    reject = jnp.sum(jnp.where(spans == 2, score, 0.0), axis=0, keepdims=True)
    part_ref[...] = jnp.concatenate([chosen, reject], axis=1) / 64.0


def attend(here, pieces, q, readout, interpret=False):
    tok, width = q.shape
    hd = pieces[0].shape[1] // 2
    n = len(pieces)
    full = lambda shape: pl.BlockSpec(shape, lambda h, here: (0, 0))
    grid_spec = pltpu.PrefetchScalarGridSpec(
        num_scalar_prefetch=1,
        grid=(1,),
        in_specs=[full(p.shape) for p in pieces]
        + [full((tok, width)), full((1, width))],
        out_specs=[full((tok, width)), full((1, 2))],
    )
    return pl.pallas_call(
        attend_kernel,
        grid_spec=grid_spec,
        out_shape=[
            jax.ShapeDtypeStruct((tok, width), jnp.bfloat16),
            jax.ShapeDtypeStruct((1, 2), jnp.float32),
        ],
        compiler_params=pltpu.CompilerParams(dimension_semantics=("arbitrary",)),
        interpret=interpret,
    )(here, *pieces, q, readout)


def gathered(value, axes):
    count = lax.axis_size(axes)
    copies = jnp.broadcast_to(value[None], (count,) + value.shape)
    return lax.all_to_all(copies, axes, 0, 0, tiled=False)


def per_device(queries, keys, values, segment_ids, span_ids, readout):
    tok = queries.shape[1]
    head_dim = keys.shape[2]
    n_ctx = lax.axis_size("ctx")
    back = min((MAX_SEGMENT - 1 + tok - 1) // tok, n_ctx - 1)
    here = lax.axis_index("ctx")
    qseg = segment_ids[0]

    kv = jnp.concatenate([keys[0], values[0]], axis=1)
    ids = jnp.stack([qseg, span_ids[0]]).astype(jnp.bfloat16)
    segrow = jnp.concatenate([ids, jnp.zeros((14, tok), jnp.bfloat16)], axis=0)
    segrow = jnp.pad(segrow, ((0, 0), (0, 2 * head_dim - tok))) if tok < 2 * head_dim else segrow[:, : 2 * head_dim]
    packed = jnp.concatenate([kv, segrow], axis=0)
    pieces = []
    for d in range(back, 0, -1):
        pairs = [(i, i + d) for i in range(n_ctx - d)]
        pieces.append(lax.ppermute(packed, "ctx", pairs))
    pieces.append(packed)

    attended, part = attend(
        jnp.reshape(here, (1,)).astype(jnp.int32), pieces, queries[0], readout[None, :]
    )
    span_scores = gathered(part[0], ("phase", "ctx")).sum(0)
    every = gathered(span_scores, "dp")
    pair_loss = jnp.mean(jax.nn.softplus(-(every[:, 0] - every[:, 1])))
    return (attended[None], span_scores[None], pair_loss)


def solution(mesh):
    in_specs = (
        P("dp", "ctx", "phase"),
        P("dp", "ctx", "phase"),
        P("dp", "ctx", "phase"),
        P("dp", "ctx"),
        P("dp", "ctx"),
        P("phase"),
    )
    out_specs = (P("dp", "ctx", "phase"), P("dp", None), P())
    return jax.shard_map(
        per_device, mesh=mesh, in_specs=in_specs, out_specs=out_specs, check_vma=False
    )
```
